256 devices in a mesh: row: 32 (over y, x, core), col: 8 (over z).
Axes of the slice: x: 4, y: 4, z: 8, core: 2. Of those that a mesh axis runs over, the one named last changes fastest.
Arguments:
- covariance: float32 [8192, 8192], P('row', 'col'), may hold values from 0 to 4, as said below
- panels: int32 [4], replicated, may hold values from 0 to 31, as said below
- observed: float32 [8192], P('row'), may hold values from -6 to 6
- drift_basis: float32 [64, 8192], P(None, 'row'), may hold values from -1.5 to 1.5
Outputs:
- complement: float32 [8192, 8192], P('row', 'col')
- factor: float32 [8192, 1024], P('row')
- solved_data: float32 [8192], P('row')
- solved_drift: float32 [64, 8192], P(None, 'row')
The draws below stay inside these ranges and needn't reach their ends.
Inputs may be any that keep to these rules, and one draw needn't show every extreme that they name: `covariance`: symmetric and positive definite. `panels`: 4 different tile indices; tile 32 - 1 is always among them.
All inputs are finite; a program needn't handle non-finite values.
Results may differ from the reference program's by a relative error of at most 0.0003.
Values sent between devices are 32-bit elements; how exact they have to be, the bound alone decides.
No kernel may reach another device: no remote copies, remote signals or barrier semaphores. Data moves between devices by JAX's collectives and lax.ppermute only.
A program may use at most 64 MiB of HBM per device.

```python
import math
import jax
import jax.numpy as jnp
from jax import lax

B = 256
DR = 64
K = 4
NT = 32
NS = 8192


def site_points(key):
    lattice = jax.random.randint(jax.random.fold_in(key, 11), (NS, 2), 0, 4096)
    return lattice.astype(jnp.float32) * (1.0 / 4096.0)


def draw_covariance(key, part):
    points = site_points(key)
    corr_range = 0.05
    nugget = jnp.exp(jax.random.uniform(jax.random.fold_in(key, 12), (NS,), jnp.float32, math.log(0.3), math.log(1.5)))
    delta_x = points[:, 0][:, None] - points[:, 0][None, :]
    delta_y = points[:, 1][:, None] - points[:, 1][None, :]
    scaled = jnp.sqrt(delta_x * delta_x + delta_y * delta_y) * (math.sqrt(3.0) / corr_range)
    matern = (1.0 + scaled) * jnp.exp(-scaled)
    return (matern + jnp.diag(nugget)).astype(jnp.float32)


def draw_drift_basis(key, part):
    points = site_points(key)
    freqs = jax.random.normal(jax.random.fold_in(key, 21), (DR, 2), jnp.float32) * 4.0
    phases = jax.random.uniform(jax.random.fold_in(key, 22), (DR, 1), jnp.float32, 0.0, 2.0 * math.pi)
    angles = 2.0 * math.pi * (freqs[:, 0:1] * points[:, 0][None, :] + freqs[:, 1:2] * points[:, 1][None, :]) + phases
    return (math.sqrt(2.0) * jnp.cos(angles)).astype(jnp.float32)


def draw_panels(key, part):
    others = jax.random.permutation(jax.random.fold_in(key, 31), NT - 1)[:K - 1]
    chosen = jnp.concatenate([others.astype(jnp.int32), jnp.full((1,), NT - 1, jnp.int32)])
    shuffle = jax.random.permutation(jax.random.fold_in(key, 32), K)
    return chosen[shuffle].astype(jnp.int32)


def level_of(key, shape, pieces, smallest, largest):
    def one(dim, shards_of):
        heights = jax.random.uniform(jax.random.fold_in(jax.random.fold_in(key, 6), dim), (shards_of,), jnp.float32, smallest / len(pieces), largest / len(pieces))
        return jnp.repeat(jnp.exp(heights), shape[dim] // shards_of).reshape((-1,) + (1,) * (len(shape) - dim - 1))

    level = one(*pieces[0])
    for cut in pieces[1:]:
        level = level * one(*cut)
    return level


def noise(key, extent, scale, limit, cuts=(), held_as=jnp.bfloat16):
    factor_of = level_of(key, extent, cuts, -0.22, 0.18) if cuts else 1.0
    array = jax.random.normal(key, extent, jnp.float32) * scale * factor_of
    return jnp.minimum(jnp.maximum(array, -limit), limit).astype(held_as)


def setup_inputs(seed: int = 0) -> dict:
    keys = jax.random.split(jax.random.key(seed), 5)
    covariance = draw_covariance(jax.random.fold_in(keys[4], 71), 0)
    panels = draw_panels(jax.random.fold_in(keys[4], 71), 0)
    observed = noise(keys[2], (NS,), 1.0, 6.0, ((0, 32),), jnp.float32)
    drift_basis = draw_drift_basis(jax.random.fold_in(keys[4], 71), 0)
    return {"covariance": covariance, "panels": panels, "observed": observed, "drift_basis": drift_basis}


def solve_right(chol_tile, values):
    return lax.linalg.triangular_solve(chol_tile, values, left_side=False, lower=True, transpose_a=True)

def reference(covariance, panels, observed, drift_basis):
    sites = covariance.shape[0]
    tile_ids = lax.iota(jnp.int32, sites) // B
    matrix = covariance
    sides = jnp.concatenate([observed[None, :], drift_basis], axis=0)
    factors = []
    for position in range(K):
        target = panels[position]
        offset = (target * B).astype(jnp.int32)
        keep = jnp.all(tile_ids[:, None] != panels[:position][None, :], axis=1).astype(matrix.dtype)
        column = lax.dynamic_slice_in_dim(matrix, offset, B, 1)
        diag_tile = lax.dynamic_slice_in_dim(column, offset, B, 0)
        chol_tile = jnp.linalg.cholesky(diag_tile)
        panel = solve_right(chol_tile, column) * keep[:, None]
        matrix = matrix - lax.dot_general(panel, panel, (((1,), (1,)), ((), ())), precision=lax.Precision.HIGHEST)
        side_tile = lax.dynamic_slice_in_dim(sides, offset, B, 1)
        solved = solve_right(chol_tile, side_tile)
        sides = sides - lax.dot_general(solved, panel, (((1,), (1,)), ((), ())), precision=lax.Precision.HIGHEST)
        placed = lax.dynamic_update_slice_in_dim(jnp.zeros_like(sides), solved, offset, 1)
        sides = jnp.where((tile_ids == target)[None, :], placed, sides)
        factors.append(panel)
    keep_all = jnp.all(tile_ids[:, None] != panels[None, :], axis=1).astype(matrix.dtype)
    complement = matrix * keep_all[:, None] * keep_all[None, :]
    return (complement, jnp.concatenate(factors, axis=1), sides[0], sides[1:])
```

```python
import jax
import jax.numpy as jnp
from jax import lax
from jax.sharding import PartitionSpec as P

B = 256
K = 4

HIGH = lax.Precision.HIGHEST


def keep_mask(tiles, chosen):
    return jnp.all(tiles[:, None] != chosen[None, :], axis=1).astype(jnp.float32)


def dot(a, b):
    return lax.dot_general(a, b, (((1,), (0,)), ((), ())), precision=HIGH)


def dot_nt(a, b):
    return lax.dot_general(a, b, (((1,), (1,)), ((), ())), precision=HIGH)


def panel_keep(tiles, panels):
    cols = []
    for p in range(K):
        cols.append(jnp.broadcast_to(keep_mask(tiles, panels[:p])[:, None], (tiles.shape[0], B)))
    return jnp.concatenate(cols, axis=1)


def on_device(covariance, panels, observed, drift_basis):
    rows_here = covariance.shape[0]
    cols_here = covariance.shape[1]
    r = lax.axis_index("row")
    row_start = r * rows_here
    col_start = lax.axis_index("col") * cols_here
    row_tiles = (row_start + lax.iota(jnp.int32, rows_here)) // B
    col_tiles = (col_start + lax.iota(jnp.int32, cols_here)) // B
    sides = jnp.concatenate([observed[None, :], drift_basis], axis=0)

    with jax.named_scope("gather_row_strip"):
        strip = lax.all_gather(covariance, "col", axis=1, tiled=True)
        panel_cols = jnp.concatenate(
            [lax.dynamic_slice_in_dim(strip, panels[j] * B, B, 1) for j in range(K)], axis=1
        )

    with jax.named_scope("share_panel_rows"):
        s_rows, a_rows, w_cols = [], [], []
        for j in range(K):
            off = panels[j] * B - row_start
            mine = (off >= 0) & (off < rows_here)
            off = jnp.clip(off, 0, rows_here - B)
            s_rows.append(jnp.where(mine, lax.dynamic_slice_in_dim(panel_cols, off, B, 0), 0.0))
            a_rows.append(jnp.where(mine, lax.dynamic_slice_in_dim(covariance, off, B, 0), 0.0))
            w_cols.append(jnp.where(mine, lax.dynamic_slice_in_dim(sides, off, B, 1), 0.0))
        rows_buf = jnp.concatenate(
            [jnp.concatenate(s_rows, axis=0), jnp.concatenate(a_rows, axis=0)], axis=1
        )
        w_buf = jnp.concatenate(w_cols, axis=1)
        rows_buf, w_buf = lax.psum((rows_buf, w_buf), "row")
        s_full = rows_buf[:, : K * B]
        a_panel_rows = rows_buf[:, K * B :]

    with jax.named_scope("block_cholesky"):
        chol = jnp.linalg.cholesky(s_full)

    with jax.named_scope("forward_solves"):
        rhs = jnp.concatenate([panel_cols, w_buf], axis=0)
        solved = lax.linalg.triangular_solve(
            chol, rhs, left_side=False, lower=True, transpose_a=True
        )
        factor_rows = solved[:rows_here] * panel_keep(row_tiles, panels)
        z = solved[rows_here:]
        factor_cols_t = lax.linalg.triangular_solve(
            chol, a_panel_rows, left_side=True, lower=True, transpose_a=False
        ) * panel_keep(col_tiles, panels).T

    with jax.named_scope("complement_update"):
        final_rows = keep_mask(row_tiles, panels)
        final_cols = keep_mask(col_tiles, panels)
        complement = (covariance - dot(factor_rows, factor_cols_t)) * final_rows[:, None] * final_cols[None, :]

    with jax.named_scope("sides_update"):
        new_sides = sides - dot_nt(z, factor_rows)
        for j in range(K):
            off = panels[j] * B - row_start
            placed = lax.dynamic_update_slice_in_dim(
                jnp.zeros_like(new_sides), z[:, j * B : (j + 1) * B], jnp.clip(off, 0, rows_here - B), 1
            )
            new_sides = jnp.where((row_tiles == panels[j])[None, :], placed, new_sides)

    return (complement, factor_rows, new_sides[0], new_sides[1:])


def solution(mesh):
    return jax.shard_map(
        on_device,
        mesh=mesh,
        in_specs=(P("row", "col"), P(), P("row"), P(None, "row")),
        out_specs=(P("row", "col"), P("row", None), P("row"), P(None, "row")),
        check_vma=False,
    )
```

```python
import jax
import jax.numpy as jnp
from jax import lax
from jax.sharding import PartitionSpec as P
from jax.experimental import pallas as pl
from jax.experimental.pallas import tpu as pltpu

B = 256
K = 4

HIGH = lax.Precision.HIGHEST


def keep_mask(tiles, chosen):
    return jnp.all(tiles[:, None] != chosen[None, :], axis=1).astype(jnp.float32)


def dot(a, b):
    return lax.dot_general(a, b, (((1,), (0,)), ((), ())), precision=HIGH)


def dot_nt(a, b):
    return lax.dot_general(a, b, (((1,), (1,)), ((), ())), precision=HIGH)


NB = 128


def chol_inv_kernel(d_ref, out_ref):
    n = d_ref.shape[0]
    rows = lax.broadcasted_iota(jnp.int32, (n, n), 0)
    cols = lax.broadcasted_iota(jnp.int32, (n, n), 1)
    out_ref[:n, :] = d_ref[...]
    out_ref[n:, :] = (rows == cols).astype(jnp.float32)
    lane = lax.broadcasted_iota(jnp.int32, (1, n), 1)
    row2 = lax.broadcasted_iota(jnp.int32, (2 * n, 1), 0)
    for k in range(n):
        m = out_ref[...]
        rowk = out_ref[k : k + 1, :]
        s = lax.rsqrt(rowk[:, k : k + 1])
        col = jnp.where(row2 >= k, m[:, k : k + 1] * s, 0.0)
        rowv = jnp.where(lane > k, rowk * s, 0.0)
        m = jnp.where(lane == k, col, m - col * rowv)
        out_ref[...] = m


def chol_inv(d):
    n = d.shape[0]
    return pl.pallas_call(
        chol_inv_kernel,
        out_shape=jax.ShapeDtypeStruct((2 * n, n), jnp.float32),
        in_specs=[pl.BlockSpec(memory_space=pltpu.VMEM)],
        out_specs=pl.BlockSpec(memory_space=pltpu.VMEM),
        cost_estimate=pl.CostEstimate(flops=6 * n * n * n, bytes_accessed=12 * n * n, transcendentals=n),
    )(d)


def blocked_solve(s_mat, rhs):
    n = s_mat.shape[0]
    solved = []
    for a in range(0, n, NB):
        out = chol_inv(s_mat[:NB, :NB])
        inv_t = out[NB:]
        p_rhs = dot(rhs[:, :NB], inv_t)
        solved.append(p_rhs)
        if a + NB < n:
            p_s = dot(s_mat[NB:, :NB], inv_t)
            s_mat = s_mat[NB:, NB:] - dot_nt(p_s, p_s)
            rhs = rhs[:, NB:] - dot_nt(p_rhs, p_s)
    return jnp.concatenate(solved, axis=1)


def panel_keep(tiles, panels):
    cols = []
    for p in range(K):
        cols.append(jnp.broadcast_to(keep_mask(tiles, panels[:p])[:, None], (tiles.shape[0], B)))
    return jnp.concatenate(cols, axis=1)


def on_device(covariance, panels, observed, drift_basis):
    rows_here = covariance.shape[0]
    cols_here = covariance.shape[1]
    r = lax.axis_index("row")
    row_start = r * rows_here
    col_start = lax.axis_index("col") * cols_here
    row_tiles = (row_start + lax.iota(jnp.int32, rows_here)) // B
    col_tiles = (col_start + lax.iota(jnp.int32, cols_here)) // B
    sides = jnp.concatenate([observed[None, :], drift_basis], axis=0)

    with jax.named_scope("gather_row_strip"):
        strip = lax.all_gather(covariance, "col", axis=1, tiled=True)
        panel_cols = jnp.concatenate(
            [lax.dynamic_slice_in_dim(strip, panels[j] * B, B, 1) for j in range(K)], axis=1
        )

    with jax.named_scope("share_panel_rows"):
        s_rows, a_rows, w_cols = [], [], []
        for j in range(K):
            off = panels[j] * B - row_start
            mine = (off >= 0) & (off < rows_here)
            off = jnp.clip(off, 0, rows_here - B)
            s_rows.append(jnp.where(mine, lax.dynamic_slice_in_dim(panel_cols, off, B, 0), 0.0))
            a_rows.append(jnp.where(mine, lax.dynamic_slice_in_dim(covariance, off, B, 0), 0.0))
            w_cols.append(jnp.where(mine, lax.dynamic_slice_in_dim(sides, off, B, 1), 0.0))
        rows_buf = jnp.concatenate(
            [jnp.concatenate(s_rows, axis=0), jnp.concatenate(a_rows, axis=0)], axis=1
        )
        w_buf = jnp.concatenate(w_cols, axis=1)
        rows_buf, w_buf = lax.psum((rows_buf, w_buf), "row")
        s_full = rows_buf[:, : K * B]
        a_panel_rows = rows_buf[:, K * B :]

    with jax.named_scope("blocked_cholesky_solve"):
        rhs = jnp.concatenate([panel_cols, w_buf, a_panel_rows.T], axis=0)
        solved = blocked_solve(s_full, rhs)
        factor_rows = solved[:rows_here] * panel_keep(row_tiles, panels)
        z = solved[rows_here : rows_here + w_buf.shape[0]]
        factor_cols = solved[rows_here + w_buf.shape[0] :] * panel_keep(col_tiles, panels)

    with jax.named_scope("complement_update"):
        final_rows = keep_mask(row_tiles, panels)
        final_cols = keep_mask(col_tiles, panels)
        complement = (covariance - dot_nt(factor_rows, factor_cols)) * final_rows[:, None] * final_cols[None, :]

    with jax.named_scope("sides_update"):
        new_sides = sides - dot_nt(z, factor_rows)
        for j in range(K):
            off = panels[j] * B - row_start
            placed = lax.dynamic_update_slice_in_dim(
                jnp.zeros_like(new_sides), z[:, j * B : (j + 1) * B], jnp.clip(off, 0, rows_here - B), 1
            )
            new_sides = jnp.where((row_tiles == panels[j])[None, :], placed, new_sides)

    return (complement, factor_rows, new_sides[0], new_sides[1:])


def solution(mesh):
    return jax.shard_map(
        on_device,
        mesh=mesh,
        in_specs=(P("row", "col"), P(), P("row"), P(None, "row")),
        out_specs=(P("row", "col"), P("row", None), P("row"), P(None, "row")),
        check_vma=False,
    )
```

```python
import jax
import jax.numpy as jnp
from jax import lax
from jax.sharding import PartitionSpec as P
from jax.experimental import pallas as pl
from jax.experimental.pallas import tpu as pltpu

B = 256
K = 4

HIGH = lax.Precision.HIGHEST


def keep_mask(tiles, chosen):
    return jnp.all(tiles[:, None] != chosen[None, :], axis=1).astype(jnp.float32)


def dot(a, b):
    return lax.dot_general(a, b, (((1,), (0,)), ((), ())), precision=HIGH)


def dot_nt(a, b):
    return lax.dot_general(a, b, (((1,), (1,)), ((), ())), precision=HIGH)


NB = 128


def chol_inv_kernel(d_ref, out_ref):
    n = d_ref.shape[0]
    rows = lax.broadcasted_iota(jnp.int32, (n, n), 0)
    cols = lax.broadcasted_iota(jnp.int32, (n, n), 1)
    out_ref[:n, :] = d_ref[...]
    out_ref[n:, :] = (rows == cols).astype(jnp.float32)
    lane = lax.broadcasted_iota(jnp.int32, (1, n), 1)
    for k in range(n):
        lo = (k // 8) * 8
        hi = min(n, ((k + 8) // 8) * 8)
        rowk = out_ref[k : k + 1, :]
        s = lax.rsqrt(rowk[:, k : k + 1])
        rowv = jnp.where(lane > k, rowk * s, 0.0)
        md = out_ref[lo:n, :]
        rows_d = lax.broadcasted_iota(jnp.int32, (n - lo, 1), 0) + lo
        col_d = jnp.where(rows_d >= k, md[:, k : k + 1] * s, 0.0)
        out_ref[lo:n, :] = jnp.where(lane == k, col_d, md - col_d * rowv)
        mi = out_ref[n : n + hi, :]
        col_i = mi[:, k : k + 1] * s
        out_ref[n : n + hi, :] = jnp.where(lane == k, col_i, mi - col_i * rowv)


def chol_inv(d):
    n = d.shape[0]
    return pl.pallas_call(
        chol_inv_kernel,
        out_shape=jax.ShapeDtypeStruct((2 * n, n), jnp.float32),
        in_specs=[pl.BlockSpec(memory_space=pltpu.VMEM)],
        out_specs=pl.BlockSpec(memory_space=pltpu.VMEM),
        cost_estimate=pl.CostEstimate(flops=6 * n * n * n, bytes_accessed=12 * n * n, transcendentals=n),
    )(d)


def blocked_solve(s_mat, rhs):
    n = s_mat.shape[0]
    solved = []
    for a in range(0, n, NB):
        out = chol_inv(s_mat[:NB, :NB])
        inv_t = out[NB:]
        p_rhs = dot(rhs[:, :NB], inv_t)
        solved.append(p_rhs)
        if a + NB < n:
            p_s = dot(s_mat[NB:, :NB], inv_t)
            s_mat = s_mat[NB:, NB:] - dot_nt(p_s, p_s)
            rhs = rhs[:, NB:] - dot_nt(p_rhs, p_s)
    return jnp.concatenate(solved, axis=1)


def panel_keep(tiles, panels):
    cols = []
    for p in range(K):
        cols.append(jnp.broadcast_to(keep_mask(tiles, panels[:p])[:, None], (tiles.shape[0], B)))
    return jnp.concatenate(cols, axis=1)


def on_device(covariance, panels, observed, drift_basis):
    rows_here = covariance.shape[0]
    cols_here = covariance.shape[1]
    r = lax.axis_index("row")
    row_start = r * rows_here
    col_start = lax.axis_index("col") * cols_here
    row_tiles = (row_start + lax.iota(jnp.int32, rows_here)) // B
    col_tiles = (col_start + lax.iota(jnp.int32, cols_here)) // B
    sides = jnp.concatenate([observed[None, :], drift_basis], axis=0)

    with jax.named_scope("gather_row_strip"):
        strip = lax.all_gather(covariance, "col", axis=1, tiled=True)
        panel_cols = jnp.concatenate(
            [lax.dynamic_slice_in_dim(strip, panels[j] * B, B, 1) for j in range(K)], axis=1
        )

    with jax.named_scope("share_panel_rows"):
        s_rows, a_rows, w_cols = [], [], []
        for j in range(K):
            off = panels[j] * B - row_start
            mine = (off >= 0) & (off < rows_here)
            off = jnp.clip(off, 0, rows_here - B)
            s_rows.append(jnp.where(mine, lax.dynamic_slice_in_dim(panel_cols, off, B, 0), 0.0))
            a_rows.append(jnp.where(mine, lax.dynamic_slice_in_dim(covariance, off, B, 0), 0.0))
            w_cols.append(jnp.where(mine, lax.dynamic_slice_in_dim(sides, off, B, 1), 0.0))
        s_full, a_panel_rows, w_buf = lax.psum(
            (jnp.concatenate(s_rows, axis=0), jnp.concatenate(a_rows, axis=0), jnp.concatenate(w_cols, axis=1)),
            "row",
        )

    with jax.named_scope("blocked_cholesky_solve"):
        rhs = jnp.concatenate([panel_cols, w_buf, a_panel_rows.T], axis=0)
        solved = blocked_solve(s_full, rhs)
        factor_rows = solved[:rows_here] * panel_keep(row_tiles, panels)
        z = solved[rows_here : rows_here + w_buf.shape[0]]
        factor_cols = solved[rows_here + w_buf.shape[0] :] * panel_keep(col_tiles, panels)

    with jax.named_scope("complement_update"):
        final_rows = keep_mask(row_tiles, panels)
        final_cols = keep_mask(col_tiles, panels)
        complement = (covariance - dot_nt(factor_rows, factor_cols)) * final_rows[:, None] * final_cols[None, :]

    with jax.named_scope("sides_update"):
        new_sides = sides - dot_nt(z, factor_rows)
        for j in range(K):
            off = panels[j] * B - row_start
            placed = lax.dynamic_update_slice_in_dim(
                jnp.zeros_like(new_sides), z[:, j * B : (j + 1) * B], jnp.clip(off, 0, rows_here - B), 1
            )
            new_sides = jnp.where((row_tiles == panels[j])[None, :], placed, new_sides)

    return (complement, factor_rows, new_sides[0], new_sides[1:])


def solution(mesh):
    return jax.shard_map(
        on_device,
        mesh=mesh,
        in_specs=(P("row", "col"), P(), P("row"), P(None, "row")),
        out_specs=(P("row", "col"), P("row", None), P("row"), P(None, "row")),
        check_vma=False,
    )
```

```python
import jax
import jax.numpy as jnp
from jax import lax
from jax.sharding import PartitionSpec as P
from jax.experimental import pallas as pl
from jax.experimental.pallas import tpu as pltpu

B = 256
K = 4

HIGH = lax.Precision.HIGHEST


def keep_mask(tiles, chosen):
    return jnp.all(tiles[:, None] != chosen[None, :], axis=1).astype(jnp.float32)


def dot(a, b):
    return lax.dot_general(a, b, (((1,), (0,)), ((), ())), precision=HIGH)


def dot_nt(a, b):
    return lax.dot_general(a, b, (((1,), (1,)), ((), ())), precision=HIGH)


NB = 128


def chol_inv_kernel(d_ref, out_ref):
    n = d_ref.shape[0]
    groups = n // 8
    lane = lax.broadcasted_iota(jnp.int32, (1, n), 1)
    sub = lax.broadcasted_iota(jnp.int32, (8, 1), 0)
    top = [d_ref[8 * g : 8 * g + 8, :] for g in range(groups)]
    bottom = [(sub + 8 * g == lane).astype(jnp.float32) for g in range(groups)]
    for k in range(n):
        g0, r0 = divmod(k, 8)
        rowk = top[g0][r0 : r0 + 1, :]
        s = lax.rsqrt(rowk[:, k : k + 1])
        rowv = jnp.where(lane > k, rowk * s, 0.0)
        for g in range(g0, groups):
            blk = top[g]
            col = blk[:, k : k + 1] * s
            if g == g0:
                col = jnp.where(sub >= r0, col, 0.0)
            top[g] = jnp.where(lane == k, col, blk - col * rowv)
        for g in range(g0 + 1):
            blk = bottom[g]
            col = blk[:, k : k + 1] * s
            bottom[g] = jnp.where(lane == k, col, blk - col * rowv)
    for g in range(groups):
        out_ref[8 * g : 8 * g + 8, :] = top[g]
        out_ref[n + 8 * g : n + 8 * g + 8, :] = bottom[g]


def chol_inv(d):
    n = d.shape[0]
    return pl.pallas_call(
        chol_inv_kernel,
        out_shape=jax.ShapeDtypeStruct((2 * n, n), jnp.float32),
        in_specs=[pl.BlockSpec(memory_space=pltpu.VMEM)],
        out_specs=pl.BlockSpec(memory_space=pltpu.VMEM),
        cost_estimate=pl.CostEstimate(flops=6 * n * n * n, bytes_accessed=12 * n * n, transcendentals=n),
    )(d)


def blocked_solve(s_mat, rhs):
    n = s_mat.shape[0]
    solved = []
    for a in range(0, n, NB):
        out = chol_inv(s_mat[:NB, :NB])
        inv_t = out[NB:]
        p_rhs = dot(rhs[:, :NB], inv_t)
        solved.append(p_rhs)
        if a + NB < n:
            p_s = dot(s_mat[NB:, :NB], inv_t)
            s_mat = s_mat[NB:, NB:] - dot_nt(p_s, p_s)
            rhs = rhs[:, NB:] - dot_nt(p_rhs, p_s)
    return jnp.concatenate(solved, axis=1)


def panel_keep(tiles, panels):
    cols = []
    for p in range(K):
        cols.append(jnp.broadcast_to(keep_mask(tiles, panels[:p])[:, None], (tiles.shape[0], B)))
    return jnp.concatenate(cols, axis=1)


def on_device(covariance, panels, observed, drift_basis):
    rows_here = covariance.shape[0]
    cols_here = covariance.shape[1]
    r = lax.axis_index("row")
    row_start = r * rows_here
    col_start = lax.axis_index("col") * cols_here
    row_tiles = (row_start + lax.iota(jnp.int32, rows_here)) // B
    col_tiles = (col_start + lax.iota(jnp.int32, cols_here)) // B
    sides = jnp.concatenate([observed[None, :], drift_basis], axis=0)

    with jax.named_scope("gather_row_strip"):
        strip = lax.all_gather(covariance, "col", axis=1, tiled=True)
        panel_cols = jnp.concatenate(
            [lax.dynamic_slice_in_dim(strip, panels[j] * B, B, 1) for j in range(K)], axis=1
        )

    with jax.named_scope("share_panel_rows"):
        s_rows, a_rows, w_cols = [], [], []
        for j in range(K):
            off = panels[j] * B - row_start
            mine = (off >= 0) & (off < rows_here)
            off = jnp.clip(off, 0, rows_here - B)
            s_rows.append(jnp.where(mine, lax.dynamic_slice_in_dim(panel_cols, off, B, 0), 0.0))
            a_rows.append(jnp.where(mine, lax.dynamic_slice_in_dim(covariance, off, B, 0), 0.0))
            w_cols.append(jnp.where(mine, lax.dynamic_slice_in_dim(sides, off, B, 1), 0.0))
        s_full, a_panel_rows, w_buf = lax.psum(
            (jnp.concatenate(s_rows, axis=0), jnp.concatenate(a_rows, axis=0), jnp.concatenate(w_cols, axis=1)),
            "row",
        )

    with jax.named_scope("blocked_cholesky_solve"):
        rhs = jnp.concatenate([panel_cols, w_buf, a_panel_rows.T], axis=0)
        solved = blocked_solve(s_full, rhs)
        factor_rows = solved[:rows_here] * panel_keep(row_tiles, panels)
        z = solved[rows_here : rows_here + w_buf.shape[0]]
        factor_cols = solved[rows_here + w_buf.shape[0] :] * panel_keep(col_tiles, panels)

    with jax.named_scope("complement_update"):
        final_rows = keep_mask(row_tiles, panels)
        final_cols = keep_mask(col_tiles, panels)
        complement = (covariance - dot_nt(factor_rows, factor_cols)) * final_rows[:, None] * final_cols[None, :]

    with jax.named_scope("sides_update"):
        new_sides = sides - dot_nt(z, factor_rows)
        for j in range(K):
            off = panels[j] * B - row_start
            placed = lax.dynamic_update_slice_in_dim(
                jnp.zeros_like(new_sides), z[:, j * B : (j + 1) * B], jnp.clip(off, 0, rows_here - B), 1
            )
            new_sides = jnp.where((row_tiles == panels[j])[None, :], placed, new_sides)

    return (complement, factor_rows, new_sides[0], new_sides[1:])


def solution(mesh):
    return jax.shard_map(
        on_device,
        mesh=mesh,
        in_specs=(P("row", "col"), P(), P("row"), P(None, "row")),
        out_specs=(P("row", "col"), P("row", None), P("row"), P(None, "row")),
        check_vma=False,
    )
```

```python
import jax
import jax.numpy as jnp
from jax import lax
from jax.sharding import PartitionSpec as P
from jax.experimental import pallas as pl
from jax.experimental.pallas import tpu as pltpu

B = 256
K = 4

HIGH = lax.Precision.HIGHEST


def keep_mask(tiles, chosen):
    return jnp.all(tiles[:, None] != chosen[None, :], axis=1).astype(jnp.float32)


def dot(a, b):
    return lax.dot_general(a, b, (((1,), (0,)), ((), ())), precision=HIGH)


def dot_nt(a, b):
    return lax.dot_general(a, b, (((1,), (1,)), ((), ())), precision=HIGH)


NB = 128


def chol_inv_kernel(d_ref, out_ref):
    n = d_ref.shape[0]
    groups = n // 8
    lane = lax.broadcasted_iota(jnp.int32, (1, n), 1)
    sub = lax.broadcasted_iota(jnp.int32, (8, 1), 0)
    top = [d_ref[8 * g : 8 * g + 8, :] for g in range(groups)]
    bottom = [(sub + 8 * g == lane).astype(jnp.float32) for g in range(groups)]
    for k in range(n):
        g0, r0 = divmod(k, 8)
        rowk = top[g0][r0 : r0 + 1, :]
        s = lax.rsqrt(rowk[:, k : k + 1])
        rowv = jnp.where(lane > k, rowk * s, 0.0)
        for g in range(g0, groups):
            blk = top[g]
            col = blk[:, k : k + 1] * s
            if g == g0:
                col = jnp.where(sub >= r0, col, 0.0)
            top[g] = jnp.where(lane == k, col, blk - col * rowv)
        for g in range(g0 + 1):
            blk = bottom[g]
            col = blk[:, k : k + 1] * s
            bottom[g] = jnp.where(lane == k, col, blk - col * rowv)
    for g in range(groups):
        out_ref[8 * g : 8 * g + 8, :] = top[g]
        out_ref[n + 8 * g : n + 8 * g + 8, :] = bottom[g]


def chol_inv(d):
    n = d.shape[0]
    return pl.pallas_call(
        chol_inv_kernel,
        out_shape=jax.ShapeDtypeStruct((2 * n, n), jnp.float32),
        in_specs=[pl.BlockSpec(memory_space=pltpu.VMEM)],
        out_specs=pl.BlockSpec(memory_space=pltpu.VMEM),
        cost_estimate=pl.CostEstimate(flops=6 * n * n * n, bytes_accessed=12 * n * n, transcendentals=n),
    )(d)


def blocked_solve(s_mat, rhs, back_rows):
    n = s_mat.shape[0]
    solved, inv_ts, below = [], [], []
    for a in range(0, n, NB):
        out = chol_inv(s_mat[:NB, :NB])
        inv_t = out[NB:]
        inv_ts.append(inv_t)
        p_rhs = dot(rhs[:, :NB], inv_t)
        solved.append(p_rhs)
        if a + NB < n:
            p_s = dot(s_mat[NB:, :NB], inv_t)
            below.append(p_s)
            s_mat = s_mat[NB:, NB:] - dot_nt(p_s, p_s)
            rhs = rhs[:, NB:] - dot_nt(p_rhs, p_s)
    back = []
    for kb in reversed(range(n // NB)):
        x_k = solved[kb][:back_rows]
        if back:
            x_k = x_k - dot(jnp.concatenate(back, axis=1), below[kb])
        back.insert(0, dot_nt(x_k, inv_ts[kb]))
    return jnp.concatenate(solved, axis=1), jnp.concatenate(back, axis=1)


def panel_keep(tiles, panels):
    cols = []
    for p in range(K):
        cols.append(jnp.broadcast_to(keep_mask(tiles, panels[:p])[:, None], (tiles.shape[0], B)))
    return jnp.concatenate(cols, axis=1)


def on_device(covariance, panels, observed, drift_basis):
    rows_here = covariance.shape[0]
    cols_here = covariance.shape[1]
    r = lax.axis_index("row")
    row_start = r * rows_here
    col_start = lax.axis_index("col") * cols_here
    row_tiles = (row_start + lax.iota(jnp.int32, rows_here)) // B
    col_tiles = (col_start + lax.iota(jnp.int32, cols_here)) // B
    sides = jnp.concatenate([observed[None, :], drift_basis], axis=0)

    with jax.named_scope("gather_row_strip"):
        strip = lax.all_gather(covariance, "col", axis=1, tiled=True)
        panel_cols = jnp.concatenate(
            [lax.dynamic_slice_in_dim(strip, panels[j] * B, B, 1) for j in range(K)], axis=1
        )

    with jax.named_scope("share_panel_rows"):
        s_rows, a_rows, w_cols = [], [], []
        for j in range(K):
            off = panels[j] * B - row_start
            mine = (off >= 0) & (off < rows_here)
            off = jnp.clip(off, 0, rows_here - B)
            s_rows.append(jnp.where(mine, lax.dynamic_slice_in_dim(panel_cols, off, B, 0), 0.0))
            a_rows.append(jnp.where(mine, lax.dynamic_slice_in_dim(covariance, off, B, 0), 0.0))
            w_cols.append(jnp.where(mine, lax.dynamic_slice_in_dim(sides, off, B, 1), 0.0))
        s_full, a_panel_rows, w_buf = lax.psum(
            (jnp.concatenate(s_rows, axis=0), jnp.concatenate(a_rows, axis=0), jnp.concatenate(w_cols, axis=1)),
            "row",
        )

    with jax.named_scope("blocked_cholesky_solve"):
        rhs = jnp.concatenate([panel_cols, w_buf], axis=0)
        solved, through_inverse = blocked_solve(s_full, rhs, rows_here)
        factor_rows = solved[:rows_here] * panel_keep(row_tiles, panels)
        z = solved[rows_here:]

    with jax.named_scope("complement_update"):
        final_rows = keep_mask(row_tiles, panels)
        final_cols = keep_mask(col_tiles, panels)
        complement = (covariance - dot(through_inverse, a_panel_rows)) * final_rows[:, None] * final_cols[None, :]

    with jax.named_scope("sides_update"):
        new_sides = sides - dot_nt(z, factor_rows)
        for j in range(K):
            off = panels[j] * B - row_start
            placed = lax.dynamic_update_slice_in_dim(
                jnp.zeros_like(new_sides), z[:, j * B : (j + 1) * B], jnp.clip(off, 0, rows_here - B), 1
            )
            new_sides = jnp.where((row_tiles == panels[j])[None, :], placed, new_sides)

    return (complement, factor_rows, new_sides[0], new_sides[1:])


def solution(mesh):
    return jax.shard_map(
        on_device,
        mesh=mesh,
        in_specs=(P("row", "col"), P(), P("row"), P(None, "row")),
        out_specs=(P("row", "col"), P("row", None), P("row"), P(None, "row")),
        check_vma=False,
    )
```

```python
import jax
import jax.numpy as jnp
from jax import lax
from jax.sharding import PartitionSpec as P
from jax.experimental import pallas as pl
from jax.experimental.pallas import tpu as pltpu

B = 256
K = 4

HIGH = lax.Precision.HIGHEST


def keep_mask(tiles, chosen):
    return jnp.all(tiles[:, None] != chosen[None, :], axis=1).astype(jnp.float32)


def dot(a, b):
    return lax.dot_general(a, b, (((1,), (0,)), ((), ())), precision=HIGH)


def dot_nt(a, b):
    return lax.dot_general(a, b, (((1,), (1,)), ((), ())), precision=HIGH)


NB = 128


def chol_inv_kernel(d_ref, out_ref):
    n = d_ref.shape[0]
    groups = n // 8
    lane = lax.broadcasted_iota(jnp.int32, (1, n), 1)
    sub = lax.broadcasted_iota(jnp.int32, (8, 1), 0)
    top = [d_ref[8 * g : 8 * g + 8, :] for g in range(groups)]
    bottom = [(sub + 8 * g == lane).astype(jnp.float32) for g in range(groups)]
    for k in range(n):
        g0, r0 = divmod(k, 8)
        rowk = top[g0][r0 : r0 + 1, :]
        s = lax.rsqrt(rowk[:, k : k + 1])
        rowv = jnp.where(lane > k, rowk * s, 0.0)
        for g in range(g0, groups):
            blk = top[g]
            col = blk[:, k : k + 1] * s
            if g == g0:
                col = jnp.where(sub >= r0, col, 0.0)
            top[g] = jnp.where(lane == k, col, blk - col * rowv)
        for g in range(g0 + 1):
            blk = bottom[g]
            col = blk[:, k : k + 1] * s
            bottom[g] = jnp.where(lane == k, col, blk - col * rowv)
    for g in range(groups):
        out_ref[8 * g : 8 * g + 8, :] = top[g]
        out_ref[n + 8 * g : n + 8 * g + 8, :] = bottom[g]


def chol_inv(d):
    n = d.shape[0]
    return pl.pallas_call(
        chol_inv_kernel,
        out_shape=jax.ShapeDtypeStruct((2 * n, n), jnp.float32),
        in_specs=[pl.BlockSpec(memory_space=pltpu.VMEM)],
        out_specs=pl.BlockSpec(memory_space=pltpu.VMEM),
        cost_estimate=pl.CostEstimate(flops=6 * n * n * n, bytes_accessed=12 * n * n, transcendentals=n),
    )(d)


def blocked_solve(s_mat, rhs, back_rows):
    n = s_mat.shape[0]
    solved, inv_ts, below = [], [], []
    for a in range(0, n, NB):
        out = chol_inv(s_mat[:NB, :NB])
        inv_t = out[NB:]
        inv_ts.append(inv_t)
        p_rhs = dot(rhs[:, :NB], inv_t)
        solved.append(p_rhs)
        if a + NB < n:
            p_s = dot(s_mat[NB:, :NB], inv_t)
            below.append(p_s)
            s_mat = s_mat[NB:, NB:] - dot_nt(p_s, p_s)
            rhs = rhs[:, NB:] - dot_nt(p_rhs, p_s)
    back = []
    for kb in reversed(range(n // NB)):
        x_k = solved[kb][:back_rows]
        if back:
            x_k = x_k - dot(jnp.concatenate(back, axis=1), below[kb])
        back.insert(0, dot_nt(x_k, inv_ts[kb]))
    return jnp.concatenate(solved, axis=1), jnp.concatenate(back, axis=1)


def panel_keep(tiles, panels):
    cols = []
    for p in range(K):
        cols.append(jnp.broadcast_to(keep_mask(tiles, panels[:p])[:, None], (tiles.shape[0], B)))
    return jnp.concatenate(cols, axis=1)


def on_device(covariance, panels, observed, drift_basis):
    rows_here = covariance.shape[0]
    cols_here = covariance.shape[1]
    r = lax.axis_index("row")
    row_start = r * rows_here
    col_start = lax.axis_index("col") * cols_here
    row_tiles = (row_start + lax.iota(jnp.int32, rows_here)) // B
    col_tiles = (col_start + lax.iota(jnp.int32, cols_here)) // B
    sides = jnp.concatenate([observed[None, :], drift_basis], axis=0)

    with jax.named_scope("gather_panel_columns"):
        pieces = []
        for j in range(K):
            off = panels[j] * B - col_start
            mine = (off >= 0) & (off < cols_here)
            tile = lax.dynamic_slice_in_dim(covariance, jnp.clip(off, 0, cols_here - B), B, 1)
            pieces.append(jnp.where(mine, tile, 0.0))
        panel_cols = lax.psum(jnp.concatenate(pieces, axis=1), "col")

    with jax.named_scope("share_panel_rows"):
        s_rows, a_rows, w_cols = [], [], []
        for j in range(K):
            off = panels[j] * B - row_start
            mine = (off >= 0) & (off < rows_here)
            off = jnp.clip(off, 0, rows_here - B)
            s_rows.append(jnp.where(mine, lax.dynamic_slice_in_dim(panel_cols, off, B, 0), 0.0))
            a_rows.append(jnp.where(mine, lax.dynamic_slice_in_dim(covariance, off, B, 0), 0.0))
            w_cols.append(jnp.where(mine, lax.dynamic_slice_in_dim(sides, off, B, 1), 0.0))
        s_full, a_panel_rows, w_buf = lax.psum(
            (jnp.concatenate(s_rows, axis=0), jnp.concatenate(a_rows, axis=0), jnp.concatenate(w_cols, axis=1)),
            "row",
        )

    with jax.named_scope("blocked_cholesky_solve"):
        rhs = jnp.concatenate([panel_cols, w_buf], axis=0)
        solved, through_inverse = blocked_solve(s_full, rhs, rows_here)
        factor_rows = solved[:rows_here] * panel_keep(row_tiles, panels)
        z = solved[rows_here:]

    with jax.named_scope("complement_update"):
        final_rows = keep_mask(row_tiles, panels)
        final_cols = keep_mask(col_tiles, panels)
        complement = (covariance - dot(through_inverse, a_panel_rows)) * final_rows[:, None] * final_cols[None, :]

    with jax.named_scope("sides_update"):
        new_sides = sides - dot_nt(z, factor_rows)
        for j in range(K):
            off = panels[j] * B - row_start
            placed = lax.dynamic_update_slice_in_dim(
                jnp.zeros_like(new_sides), z[:, j * B : (j + 1) * B], jnp.clip(off, 0, rows_here - B), 1
            )
            new_sides = jnp.where((row_tiles == panels[j])[None, :], placed, new_sides)

    return (complement, factor_rows, new_sides[0], new_sides[1:])


def solution(mesh):
    return jax.shard_map(
        on_device,
        mesh=mesh,
        in_specs=(P("row", "col"), P(), P("row"), P(None, "row")),
        out_specs=(P("row", "col"), P("row", None), P("row"), P(None, "row")),
        check_vma=False,
    )
```

```python
import jax
import jax.numpy as jnp
from jax import lax
from jax.sharding import PartitionSpec as P
from jax.experimental import pallas as pl
from jax.experimental.pallas import tpu as pltpu

B = 256
K = 4

HIGH = lax.Precision.HIGHEST


def keep_mask(tiles, chosen):
    return jnp.all(tiles[:, None] != chosen[None, :], axis=1).astype(jnp.float32)


def dot(a, b):
    return lax.dot_general(a, b, (((1,), (0,)), ((), ())), precision=HIGH)


def dot_nt(a, b):
    return lax.dot_general(a, b, (((1,), (1,)), ((), ())), precision=HIGH)


NB = 128


def chol_inv_kernel(d_ref, out_ref):
    n = d_ref.shape[0]
    groups = n // 8
    lane = lax.broadcasted_iota(jnp.int32, (1, n), 1)
    sub = lax.broadcasted_iota(jnp.int32, (8, 1), 0)
    top = [d_ref[8 * g : 8 * g + 8, :] for g in range(groups)]
    bottom = [(sub + 8 * g == lane).astype(jnp.float32) for g in range(groups)]
    for k in range(0, n, 2):
        g0, r0 = divmod(k, 8)
        row_a = top[g0][r0 : r0 + 1, :]
        row_b = top[g0][r0 + 1 : r0 + 2, :]
        s_a = lax.rsqrt(row_a[:, k : k + 1])
        l_ba = row_b[:, k : k + 1] * s_a
        s_b = lax.rsqrt(row_b[:, k + 1 : k + 2] - l_ba * l_ba)
        later = lane > k + 1
        ru = jnp.where(later, row_a * s_a, 0.0)
        rv = jnp.where(later, (row_b - l_ba * (row_a * s_a)) * s_b, 0.0)

        def step(blk, mask_a=None, mask_b=None):
            u = blk[:, k : k + 1] * s_a
            v = (blk[:, k + 1 : k + 2] - u * l_ba) * s_b
            if mask_a is not None:
                u = jnp.where(mask_a, u, 0.0)
                v = jnp.where(mask_b, v, 0.0)
            out = blk - u * ru - v * rv
            return jnp.where(lane == k, u, jnp.where(lane == k + 1, v, out))

        top[g0] = step(top[g0], sub >= r0, sub >= r0 + 1)
        for g in range(g0 + 1, groups):
            top[g] = step(top[g])
        for g in range(g0 + 1):
            bottom[g] = step(bottom[g])
    for g in range(groups):
        out_ref[8 * g : 8 * g + 8, :] = top[g]
        out_ref[n + 8 * g : n + 8 * g + 8, :] = bottom[g]


def chol_inv(d):
    n = d.shape[0]
    return pl.pallas_call(
        chol_inv_kernel,
        out_shape=jax.ShapeDtypeStruct((2 * n, n), jnp.float32),
        in_specs=[pl.BlockSpec(memory_space=pltpu.VMEM)],
        out_specs=pl.BlockSpec(memory_space=pltpu.VMEM),
        cost_estimate=pl.CostEstimate(flops=6 * n * n * n, bytes_accessed=12 * n * n, transcendentals=n),
    )(d)


def blocked_solve(s_mat, rhs, back_rows):
    n = s_mat.shape[0]
    solved, inv_ts, below = [], [], []
    for a in range(0, n, NB):
        out = chol_inv(s_mat[:NB, :NB])
        inv_t = out[NB:]
        inv_ts.append(inv_t)
        p_rhs = dot(rhs[:, :NB], inv_t)
        solved.append(p_rhs)
        if a + NB < n:
            p_s = dot(s_mat[NB:, :NB], inv_t)
            below.append(p_s)
            s_mat = s_mat[NB:, NB:] - dot_nt(p_s, p_s)
            rhs = rhs[:, NB:] - dot_nt(p_rhs, p_s)
    back = []
    for kb in reversed(range(n // NB)):
        x_k = solved[kb][:back_rows]
        if back:
            x_k = x_k - dot(jnp.concatenate(back, axis=1), below[kb])
        back.insert(0, dot_nt(x_k, inv_ts[kb]))
    return jnp.concatenate(solved, axis=1), jnp.concatenate(back, axis=1)


def panel_keep(tiles, panels):
    cols = []
    for p in range(K):
        cols.append(jnp.broadcast_to(keep_mask(tiles, panels[:p])[:, None], (tiles.shape[0], B)))
    return jnp.concatenate(cols, axis=1)


def on_device(covariance, panels, observed, drift_basis):
    rows_here = covariance.shape[0]
    cols_here = covariance.shape[1]
    r = lax.axis_index("row")
    row_start = r * rows_here
    col_start = lax.axis_index("col") * cols_here
    row_tiles = (row_start + lax.iota(jnp.int32, rows_here)) // B
    col_tiles = (col_start + lax.iota(jnp.int32, cols_here)) // B
    sides = jnp.concatenate([observed[None, :], drift_basis], axis=0)

    with jax.named_scope("gather_panel_columns"):
        pieces = []
        for j in range(K):
            off = panels[j] * B - col_start
            mine = (off >= 0) & (off < cols_here)
            tile = lax.dynamic_slice_in_dim(covariance, jnp.clip(off, 0, cols_here - B), B, 1)
            pieces.append(jnp.where(mine, tile, 0.0))
        panel_cols = lax.psum(jnp.concatenate(pieces, axis=1), "col")

    with jax.named_scope("share_panel_rows"):
        s_rows, a_rows, w_cols = [], [], []
        for j in range(K):
            off = panels[j] * B - row_start
            mine = (off >= 0) & (off < rows_here)
            off = jnp.clip(off, 0, rows_here - B)
            s_rows.append(jnp.where(mine, lax.dynamic_slice_in_dim(panel_cols, off, B, 0), 0.0))
            a_rows.append(jnp.where(mine, lax.dynamic_slice_in_dim(covariance, off, B, 0), 0.0))
            w_cols.append(jnp.where(mine, lax.dynamic_slice_in_dim(sides, off, B, 1), 0.0))
        s_full, a_panel_rows, w_buf = lax.psum(
            (jnp.concatenate(s_rows, axis=0), jnp.concatenate(a_rows, axis=0), jnp.concatenate(w_cols, axis=1)),
            "row",
        )

    with jax.named_scope("blocked_cholesky_solve"):
        rhs = jnp.concatenate([panel_cols, w_buf], axis=0)
        solved, through_inverse = blocked_solve(s_full, rhs, rows_here)
        factor_rows = solved[:rows_here] * panel_keep(row_tiles, panels)
        z = solved[rows_here:]

    with jax.named_scope("complement_update"):
        final_rows = keep_mask(row_tiles, panels)
        final_cols = keep_mask(col_tiles, panels)
        complement = (covariance - dot(through_inverse, a_panel_rows)) * final_rows[:, None] * final_cols[None, :]

    with jax.named_scope("sides_update"):
        new_sides = sides - dot_nt(z, factor_rows)
        for j in range(K):
            off = panels[j] * B - row_start
            placed = lax.dynamic_update_slice_in_dim(
                jnp.zeros_like(new_sides), z[:, j * B : (j + 1) * B], jnp.clip(off, 0, rows_here - B), 1
            )
            new_sides = jnp.where((row_tiles == panels[j])[None, :], placed, new_sides)

    return (complement, factor_rows, new_sides[0], new_sides[1:])


def solution(mesh):
    return jax.shard_map(
        on_device,
        mesh=mesh,
        in_specs=(P("row", "col"), P(), P("row"), P(None, "row")),
        out_specs=(P("row", "col"), P("row", None), P("row"), P(None, "row")),
        check_vma=False,
    )
```

```python
import jax
import jax.numpy as jnp
from jax import lax
from jax.sharding import PartitionSpec as P
from jax.experimental import pallas as pl
from jax.experimental.pallas import tpu as pltpu

B = 256
K = 4

HIGH = lax.Precision.HIGHEST


def keep_mask(tiles, chosen):
    return jnp.all(tiles[:, None] != chosen[None, :], axis=1).astype(jnp.float32)


def dot(a, b):
    return lax.dot_general(a, b, (((1,), (0,)), ((), ())), precision=HIGH)


def dot_nt(a, b):
    return lax.dot_general(a, b, (((1,), (1,)), ((), ())), precision=HIGH)


NB = 128


def chol_inv_kernel(d_ref, out_ref):
    n = d_ref.shape[0]
    groups = n // 8
    lane = lax.broadcasted_iota(jnp.int32, (1, n), 1)
    sub = lax.broadcasted_iota(jnp.int32, (8, 1), 0)
    top = [d_ref[8 * g : 8 * g + 8, :] for g in range(groups)]
    bottom = [(sub + 8 * g == lane).astype(jnp.float32) for g in range(groups)]
    for k in range(n):
        g0, r0 = divmod(k, 8)
        rowk = top[g0][r0 : r0 + 1, :]
        s = lax.rsqrt(rowk[:, k : k + 1])
        rowv = jnp.where(lane > k, rowk * s, 0.0)
        for g in range(g0, groups):
            blk = top[g]
            col = blk[:, k : k + 1] * s
            if g == g0:
                col = jnp.where(sub >= r0, col, 0.0)
            top[g] = jnp.where(lane == k, col, blk - col * rowv)
        for g in range(g0 + 1):
            blk = bottom[g]
            col = blk[:, k : k + 1] * s
            bottom[g] = jnp.where(lane == k, col, blk - col * rowv)
    for g in range(groups):
        out_ref[8 * g : 8 * g + 8, :] = bottom[g]


def chol_inv_t(s_mat):
    return pl.pallas_call(
        chol_inv_kernel,
        out_shape=jax.ShapeDtypeStruct((NB, NB), jnp.float32),
        grid=(1,),
        in_specs=[pl.BlockSpec((NB, NB), lambda i: (0, 0))],
        out_specs=pl.BlockSpec((NB, NB), lambda i: (0, 0)),
        cost_estimate=pl.CostEstimate(flops=6 * NB * NB * NB, bytes_accessed=8 * NB * NB, transcendentals=NB),
    )(s_mat)


def blocked_solve(s_mat, rhs, back_rows):
    n = s_mat.shape[0]
    solved, inv_ts, below = [], [], []
    for a in range(0, n, NB):
        inv_t = chol_inv_t(s_mat)
        inv_ts.append(inv_t)
        p_rhs = dot(rhs[:, :NB], inv_t)
        solved.append(p_rhs)
        if a + NB < n:
            p_s = dot(s_mat[NB:, :NB], inv_t)
            below.append(p_s)
            s_mat = s_mat[NB:, NB:] - dot_nt(p_s, p_s)
            rhs = rhs[:, NB:] - dot_nt(p_rhs, p_s)
    back = []
    for kb in reversed(range(n // NB)):
        x_k = solved[kb][:back_rows]
        if back:
            x_k = x_k - dot(jnp.concatenate(back, axis=1), below[kb])
        back.insert(0, dot_nt(x_k, inv_ts[kb]))
    return jnp.concatenate(solved, axis=1), jnp.concatenate(back, axis=1)


def panel_keep(tiles, panels):
    cols = []
    for p in range(K):
        cols.append(jnp.broadcast_to(keep_mask(tiles, panels[:p])[:, None], (tiles.shape[0], B)))
    return jnp.concatenate(cols, axis=1)


def on_device(covariance, panels, observed, drift_basis):
    rows_here = covariance.shape[0]
    cols_here = covariance.shape[1]
    r = lax.axis_index("row")
    row_start = r * rows_here
    col_start = lax.axis_index("col") * cols_here
    row_tiles = (row_start + lax.iota(jnp.int32, rows_here)) // B
    col_tiles = (col_start + lax.iota(jnp.int32, cols_here)) // B
    sides = jnp.concatenate([observed[None, :], drift_basis], axis=0)

    with jax.named_scope("gather_panel_columns"):
        pieces = []
        for j in range(K):
            off = panels[j] * B - col_start
            mine = (off >= 0) & (off < cols_here)
            tile = lax.dynamic_slice_in_dim(covariance, jnp.clip(off, 0, cols_here - B), B, 1)
            pieces.append(jnp.where(mine, tile, 0.0))
        panel_cols = lax.psum(jnp.concatenate(pieces, axis=1), "col")

    with jax.named_scope("share_panel_rows"):
        s_rows, a_rows, w_cols = [], [], []
        for j in range(K):
            off = panels[j] * B - row_start
            mine = (off >= 0) & (off < rows_here)
            off = jnp.clip(off, 0, rows_here - B)
            s_rows.append(jnp.where(mine, lax.dynamic_slice_in_dim(panel_cols, off, B, 0), 0.0))
            a_rows.append(jnp.where(mine, lax.dynamic_slice_in_dim(covariance, off, B, 0), 0.0))
            w_cols.append(jnp.where(mine, lax.dynamic_slice_in_dim(sides, off, B, 1), 0.0))
        s_full, a_panel_rows, w_buf = lax.psum(
            (jnp.concatenate(s_rows, axis=0), jnp.concatenate(a_rows, axis=0), jnp.concatenate(w_cols, axis=1)),
            "row",
        )

    with jax.named_scope("blocked_cholesky_solve"):
        rhs = jnp.concatenate([panel_cols, w_buf], axis=0)
        solved, through_inverse = blocked_solve(s_full, rhs, rows_here)
        factor_rows = solved[:rows_here] * panel_keep(row_tiles, panels)
        z = solved[rows_here:]

    with jax.named_scope("complement_update"):
        final_rows = keep_mask(row_tiles, panels)
        final_cols = keep_mask(col_tiles, panels)
        complement = (covariance - dot(through_inverse, a_panel_rows)) * final_rows[:, None] * final_cols[None, :]

    with jax.named_scope("sides_update"):
        new_sides = sides - dot_nt(z, factor_rows)
        for j in range(K):
            off = panels[j] * B - row_start
            placed = lax.dynamic_update_slice_in_dim(
                jnp.zeros_like(new_sides), z[:, j * B : (j + 1) * B], jnp.clip(off, 0, rows_here - B), 1
            )
            new_sides = jnp.where((row_tiles == panels[j])[None, :], placed, new_sides)

    return (complement, factor_rows, new_sides[0], new_sides[1:])


def solution(mesh):
    return jax.shard_map(
        on_device,
        mesh=mesh,
        in_specs=(P("row", "col"), P(), P("row"), P(None, "row")),
        out_specs=(P("row", "col"), P("row", None), P("row"), P(None, "row")),
        check_vma=False,
    )
```

```python
import jax
import jax.numpy as jnp
from jax import lax
from jax.sharding import PartitionSpec as P
from jax.experimental import pallas as pl
from jax.experimental.pallas import tpu as pltpu

B = 256
K = 4

HIGH = lax.Precision.HIGHEST


def keep_mask(tiles, chosen):
    return jnp.all(tiles[:, None] != chosen[None, :], axis=1).astype(jnp.float32)


def dot(a, b):
    return lax.dot_general(a, b, (((1,), (0,)), ((), ())), precision=HIGH)


def dot_nt(a, b):
    return lax.dot_general(a, b, (((1,), (1,)), ((), ())), precision=HIGH)


NB = 128


def chol_inv_kernel(d_ref, out_ref):
    n = d_ref.shape[0]
    groups = n // 8
    lane = lax.broadcasted_iota(jnp.int32, (1, n), 1)
    sub = lax.broadcasted_iota(jnp.int32, (8, 1), 0)
    top = [d_ref[8 * g : 8 * g + 8, :] for g in range(groups)]
    bottom = [(sub + 8 * g == lane).astype(jnp.float32) for g in range(groups)]
    for k in range(n):
        g0, r0 = divmod(k, 8)
        rowk = top[g0][r0 : r0 + 1, :]
        s = lax.rsqrt(rowk[:, k : k + 1])
        rowv = jnp.where(lane > k, rowk * s, 0.0)
        for g in range(g0, groups):
            blk = top[g]
            col = blk[:, k : k + 1] * s
            if g == g0:
                col = jnp.where(sub >= r0, col, 0.0)
            top[g] = jnp.where(lane == k, col, blk - col * rowv)
        for g in range(g0 + 1):
            blk = bottom[g]
            col = blk[:, k : k + 1] * s
            bottom[g] = jnp.where(lane == k, col, blk - col * rowv)
    for g in range(groups):
        out_ref[8 * g : 8 * g + 8, :] = bottom[g]


def chol_inv_t(s_mat):
    return pl.pallas_call(
        chol_inv_kernel,
        out_shape=jax.ShapeDtypeStruct((NB, NB), jnp.float32),
        grid=(1,),
        in_specs=[pl.BlockSpec((NB, NB), lambda i: (0, 0))],
        out_specs=pl.BlockSpec((NB, NB), lambda i: (0, 0)),
        cost_estimate=pl.CostEstimate(flops=6 * NB * NB * NB, bytes_accessed=8 * NB * NB, transcendentals=NB),
    )(s_mat)


def blocked_solve(s_mat, rhs, back_rows):
    n = s_mat.shape[0]
    solved, inv_ts, below = [], [], []
    for a in range(0, n, NB):
        inv_t = chol_inv_t(s_mat)
        inv_ts.append(inv_t)
        p_rhs = dot(rhs[:, :NB], inv_t)
        solved.append(p_rhs)
        if a + NB < n:
            p_s = dot(s_mat[NB:, :NB], inv_t)
            below.append(p_s)
            s_mat = s_mat[NB:, NB:] - dot_nt(p_s, p_s)
            rhs = rhs[:, NB:] - dot_nt(p_rhs, p_s)
    back = []
    for kb in reversed(range(n // NB)):
        x_k = solved[kb][:back_rows]
        if back:
            x_k = x_k - dot(jnp.concatenate(back, axis=1), below[kb])
        back.insert(0, dot_nt(x_k, inv_ts[kb]))
    return jnp.concatenate(solved, axis=1), jnp.concatenate(back, axis=1)


def panel_keep(tiles, panels):
    cols = []
    for p in range(K):
        cols.append(jnp.broadcast_to(keep_mask(tiles, panels[:p])[:, None], (tiles.shape[0], B)))
    return jnp.concatenate(cols, axis=1)


def on_device(covariance, panels, observed, drift_basis):
    rows_here = covariance.shape[0]
    cols_here = covariance.shape[1]
    r = lax.axis_index("row")
    row_start = r * rows_here
    col_start = lax.axis_index("col") * cols_here
    row_tiles = (row_start + lax.iota(jnp.int32, rows_here)) // B
    col_tiles = (col_start + lax.iota(jnp.int32, cols_here)) // B
    sides = jnp.concatenate([observed[None, :], drift_basis], axis=0)

    with jax.named_scope("gather_panel_columns"):
        pieces = []
        for j in range(K):
            off = panels[j] * B - col_start
            mine = (off >= 0) & (off < cols_here)
            tile = lax.dynamic_slice_in_dim(covariance, jnp.clip(off, 0, cols_here - B), B, 1)
            pieces.append(jnp.where(mine, tile, 0.0))
        panel_cols = lax.psum(jnp.concatenate(pieces, axis=1), "col")

    with jax.named_scope("share_panel_rows"):
        s_rows, a_rows, w_cols = [], [], []
        for j in range(K):
            off = panels[j] * B - row_start
            mine = (off >= 0) & (off < rows_here)
            off = jnp.clip(off, 0, rows_here - B)
            s_rows.append(jnp.where(mine, lax.dynamic_slice_in_dim(panel_cols, off, B, 0), 0.0))
            a_rows.append(jnp.where(mine, lax.dynamic_slice_in_dim(covariance, off, B, 0), 0.0))
            w_cols.append(jnp.where(mine, lax.dynamic_slice_in_dim(sides, off, B, 1), 0.0))
        s_full, a_panel_rows, w_buf = lax.psum(
            (jnp.concatenate(s_rows, axis=0), jnp.concatenate(a_rows, axis=0), jnp.concatenate(w_cols, axis=1)),
            "row",
        )

    with jax.named_scope("blocked_cholesky_solve"):
        rhs = jnp.concatenate([panel_cols, w_buf], axis=0)
        solved, through_inverse = blocked_solve(s_full, rhs, rows_here)
        factor_rows = solved[:rows_here] * panel_keep(row_tiles, panels)
        z = solved[rows_here:]

    with jax.named_scope("complement_update"):
        final_rows = keep_mask(row_tiles, panels)
        final_cols = keep_mask(col_tiles, panels)
        update = lax.dot_general(
            through_inverse, a_panel_rows, (((1,), (0,)), ((), ())), precision=lax.Precision.HIGH
        )
        complement = (covariance - update) * final_rows[:, None] * final_cols[None, :]

    with jax.named_scope("sides_update"):
        new_sides = sides - dot_nt(z, factor_rows)
        for j in range(K):
            off = panels[j] * B - row_start
            placed = lax.dynamic_update_slice_in_dim(
                jnp.zeros_like(new_sides), z[:, j * B : (j + 1) * B], jnp.clip(off, 0, rows_here - B), 1
            )
            new_sides = jnp.where((row_tiles == panels[j])[None, :], placed, new_sides)

    return (complement, factor_rows, new_sides[0], new_sides[1:])


def solution(mesh):
    return jax.shard_map(
        on_device,
        mesh=mesh,
        in_specs=(P("row", "col"), P(), P("row"), P(None, "row")),
        out_specs=(P("row", "col"), P("row", None), P("row"), P(None, "row")),
        check_vma=False,
    )
```
